256 devices in a mesh: seq: 16 (over z, core), mp: 16 (over y, x).
Axes of the slice: x: 4, y: 4, z: 8, core: 2. Of those that a mesh axis runs over, the one named last changes fastest.
Arguments:
- qkv_owned: bfloat16 [16, 6144, 6144], P('mp', 'seq'), may hold values from -6 to 6, as said below
- owner: int32 [16, 2048], P('mp'), may hold values from 0 to 15, as said below
- band_rows: int32 [16, 16, 4], P('mp'), may hold values from 0 to 15, as said below
- band_cols: int32 [16, 16, 4], P('mp'), may hold values from 0 to 15
- bias: float32 [16, 2], replicated, may hold values from -1.5 to 1.5
- grad_out: bfloat16 [16, 2048, 2048], P('mp', 'seq'), may hold values from -6 to 6
Outputs:
- attended: bfloat16 [16, 2048, 2048], P('mp', 'seq')
- grad_qkv: bfloat16 [16, 6144, 6144], P('mp', 'seq')
- grad_bias: float32 [16, 2], P('seq')
The draws below stay inside these ranges and needn't reach their ends.
Inputs may be any that keep to these rules, and one draw needn't show every extreme that they name: Within the 128 positions p * 128 to p * 128 + 127 of a document, at most 24 name one owner, and in every such shard some owner is named exactly 24 times. band_rows[b, 0] is b; the 8 blocks of band_rows[b] and band_cols[b] are distinct. `qkv_owned`: rows that no position names are not read.
All inputs are finite; a program needn't handle non-finite values.
Results may differ from the reference program's by a relative error of at most 0.04.
Values may be sent and summed in bfloat16 or wider, within the bound.
No kernel may reach another device: no remote copies, remote signals or barrier semaphores. Data moves between devices by JAX's collectives and lax.ppermute only.
A program may use at most 128 MiB of HBM per device.

```python
import math
import jax
import jax.numpy as jnp
from jax import lax

HEADS = 16
HEAD_DIM = 128
TOK_DEV = 128
BLOCK = 128
ROW_BLOCKS = 4
COL_BLOCKS = 4
SEQ_LEN = 2048
NBLK = 16
CAP_PAIR = 24
OWN_SLOTS = 384
DOCS = 16
FEAT = 6144
N_SEQ = 16


def owner_table(key):
    keys = jax.random.split(jax.random.fold_in(key, 17), 4)
    candidates = N_SEQ * CAP_PAIR
    cand_owner = jnp.arange(candidates, dtype=jnp.int32) // CAP_PAIR
    prefer = jax.random.randint(keys[0], (DOCS, 1, N_SEQ), 0, 2048)
    noise = jax.random.randint(keys[1], (DOCS, N_SEQ, candidates), 0, 1024)
    forced = jax.random.randint(keys[2], (DOCS, N_SEQ, 1), 0, N_SEQ)
    logit_scores = noise + jnp.take(prefer, cand_owner, axis=2)
    logit_scores = logit_scores + jnp.where(cand_owner[None, None, :] == forced, 4096, 0)
    logit_scores = logit_scores * candidates + jnp.arange(candidates, dtype=jnp.int32)
    chosen = jnp.argsort(-logit_scores, axis=-1)[:, :, :TOK_DEV]
    owners = jnp.take(cand_owner, chosen)
    mixing = jax.random.randint(keys[3], (DOCS, N_SEQ, TOK_DEV), 0, 1 << 20) * TOK_DEV + jnp.arange(TOK_DEV, dtype=jnp.int32)
    shuffle = jnp.argsort(mixing, axis=-1)
    return jnp.take_along_axis(owners, shuffle, axis=-1).reshape(DOCS, SEQ_LEN).astype(jnp.int32)


def band_table(key):
    noise = jax.random.randint(jax.random.fold_in(key, 29), (DOCS, NBLK, NBLK), 0, 1 << 16) * NBLK + jnp.arange(NBLK, dtype=jnp.int32)
    diagonal = jnp.arange(NBLK)[:, None] == jnp.arange(NBLK)[None, :]
    noise = jnp.where(diagonal[None], -1, noise)
    return jnp.argsort(noise, axis=-1)[:, :, :ROW_BLOCKS + COL_BLOCKS].astype(jnp.int32)


def draw_owner(key, part):
    return owner_table(key)


def draw_band_rows(key, part):
    return band_table(key)[:, :, :ROW_BLOCKS]


def draw_band_cols(key, part):
    return band_table(key)[:, :, ROW_BLOCKS:]


def draw_qkv_owned(key, part):
    keys = jax.random.split(jax.random.fold_in(key, 41), 2)
    total = N_SEQ * OWN_SLOTS
    shape = (DOCS, total, 3, HEADS, HEAD_DIM)
    values = jnp.clip(jax.random.normal(keys[1], shape), -6.0, 6.0)
    return values.reshape(DOCS, total, FEAT).astype(jnp.bfloat16)


def shard_levels(rng, extent, cuts, least, largest):
    def one(position, blocks):
        steps = jax.random.uniform(jax.random.fold_in(jax.random.fold_in(rng, 6), position), (blocks,), jnp.float32, least / len(cuts), largest / len(cuts))
        return jnp.repeat(jnp.exp(steps), extent[position] // blocks).reshape((-1,) + (1,) * (len(extent) - position - 1))

    gain = one(*cuts[0])
    for cut in cuts[1:]:
        gain = gain * one(*cut)
    return gain


def centred(rng, dims, spread, most, cuts=(), held_as=jnp.bfloat16):
    gain = shard_levels(rng, dims, cuts, -0.22, 0.18) if cuts else 1.0
    values = jax.random.normal(rng, dims, jnp.float32) * spread * gain
    return jnp.minimum(jnp.maximum(values, -most), most).astype(held_as)


def setup_inputs(seed: int = 0) -> dict:
    splits = jax.random.split(jax.random.key(seed), 7)
    return {
        "qkv_owned": draw_qkv_owned(jax.random.fold_in(splits[6], 71), 0),
        "owner": draw_owner(jax.random.fold_in(splits[6], 71), 0),
        "band_rows": draw_band_rows(jax.random.fold_in(splits[6], 71), 0),
        "band_cols": draw_band_cols(jax.random.fold_in(splits[6], 71), 0),
        "bias": jnp.clip(jax.random.uniform(splits[4], (HEADS, 2), jnp.float32, -1.5, 1.5), -1.5, 1.5),
        "grad_out": centred(splits[5], (DOCS, SEQ_LEN, HEADS * HEAD_DIM), 1.0, 6.0, ((0, 16), (1, 16))),
    }


def source_rows(owner_doc):
    owner_ids = jnp.arange(N_SEQ, dtype=jnp.int32)
    onehot = (owner_doc[:, None] == owner_ids[None, :]).astype(jnp.int32)
    running = jnp.cumsum(onehot, axis=0) - onehot
    return (owner_doc * OWN_SLOTS + lax.optimization_barrier(jnp.sum(running * onehot, axis=1))).astype(jnp.int32)

def blocked(array):
    return array.reshape(NBLK, BLOCK, HEAD_DIM)

def head_core(query, key_rows, value_rows, grad_rows, selected, bias_pair):
    score_scaling = 1.0 / math.sqrt(HEAD_DIM)
    num_sel = ROW_BLOCKS + COL_BLOCKS
    highest_precision = lax.Precision.HIGHEST
    query_tile_block = blocked(query).astype(jnp.float32)
    gradient_per_block = blocked(grad_rows).astype(jnp.float32)
    selected_keys = blocked(key_rows)[selected].reshape(NBLK, num_sel * BLOCK, HEAD_DIM).astype(jnp.float32)
    selected_values = blocked(value_rows)[selected].reshape(NBLK, num_sel * BLOCK, HEAD_DIM).astype(jnp.float32)
    col_kind = jnp.arange(num_sel * BLOCK) >= ROW_BLOCKS * BLOCK
    key_offset_bias = jnp.where(col_kind, bias_pair[1], bias_pair[0])
    logit_scores = jnp.einsum('xtc,xzc->xtz', query_tile_block, selected_keys, precision=highest_precision) * score_scaling + key_offset_bias[None, None, :]
    row_max = lax.optimization_barrier(jnp.max(logit_scores, axis=-1, keepdims=True))
    exp_scores = jnp.exp(logit_scores - row_max)
    weights = exp_scores / lax.optimization_barrier(jnp.sum(exp_scores, axis=-1, keepdims=True))
    reduced_weights = lax.optimization_barrier(weights.astype(jnp.bfloat16)).astype(jnp.float32)
    attention_result = jnp.einsum('ufn,unp->ufp', reduced_weights, selected_values, precision=highest_precision).astype(jnp.bfloat16)
    attn_wide = lax.optimization_barrier(attention_result).astype(jnp.float32)
    row_delta = lax.optimization_barrier(jnp.sum(gradient_per_block * attn_wide, axis=-1, keepdims=True))
    probability_gradient = jnp.einsum('xtc,xzc->xtz', gradient_per_block, selected_values, precision=highest_precision)
    dscore = weights * (probability_gradient - row_delta)
    bias_grad = jnp.stack([jnp.sum(jnp.where(col_kind, 0.0, dscore)), jnp.sum(jnp.where(col_kind, dscore, 0.0))])
    score_gradient_reduced = lax.optimization_barrier(dscore.astype(jnp.bfloat16)).astype(jnp.float32)
    query_gradient = jnp.einsum('ufn,unp->ufp', score_gradient_reduced, selected_keys, precision=highest_precision) * score_scaling
    selected_key_gradient = jnp.einsum('jyt,jyu->jtu', score_gradient_reduced, query_tile_block, precision=highest_precision) * score_scaling
    selected_value_gradient = jnp.einsum('jyt,jyu->jtu', reduced_weights, gradient_per_block, precision=highest_precision)
    block_hot = (selected[:, :, None] == jnp.arange(NBLK, dtype=jnp.int32)[None, None, :]).astype(jnp.float32)
    grad_key = jnp.einsum('bjc,bjtd->ctd', block_hot, selected_key_gradient.reshape(NBLK, num_sel, BLOCK, HEAD_DIM), precision=highest_precision)
    grad_value = jnp.einsum('bjc,bjtd->ctd', block_hot, selected_value_gradient.reshape(NBLK, num_sel, BLOCK, HEAD_DIM), precision=highest_precision)
    return (attention_result.reshape(SEQ_LEN, HEAD_DIM), query_gradient.reshape(SEQ_LEN, HEAD_DIM), grad_key.reshape(SEQ_LEN, HEAD_DIM), grad_value.reshape(SEQ_LEN, HEAD_DIM), bias_grad)

def reference(qkv_owned, owner, band_rows, band_cols, bias, grad_out):

    def one_doc(bundle):
        rows_owned, owner_doc, row_list, col_list, grad_doc = bundle
        source = source_rows(owner_doc)
        gathered = jnp.take(rows_owned, source, axis=0).reshape(SEQ_LEN, 3, HEADS, HEAD_DIM)
        selected = jnp.concatenate([row_list, col_list], axis=1)
        per_head = gathered.transpose(2, 1, 0, 3)
        grad_heads = grad_doc.reshape(SEQ_LEN, HEADS, HEAD_DIM).transpose(1, 0, 2)

        def one_head(entry):
            head_rows, head_grad, bias_pair = entry
            return head_core(head_rows[0], head_rows[1], head_rows[2], head_grad, selected, bias_pair)
        attention_result, query_gradient, grad_key, grad_value, bias_grad = lax.map(one_head, (per_head, grad_heads, bias))
        attended_doc = attention_result.transpose(1, 0, 2).reshape(SEQ_LEN, HEADS * HEAD_DIM)
        grad_all = jnp.stack([query_gradient, grad_key, grad_value], axis=0)
        grad_all = grad_all.transpose(2, 0, 1, 3).reshape(SEQ_LEN, FEAT).astype(jnp.bfloat16)
        owned = jnp.zeros((N_SEQ * OWN_SLOTS, FEAT), jnp.bfloat16).at[source].set(grad_all)
        return (attended_doc, owned, bias_grad)
    attended, grad_qkv, bias_grad = lax.map(one_doc, (qkv_owned, owner, band_rows, band_cols, grad_out))
    return (attended, grad_qkv, lax.optimization_barrier(jnp.sum(bias_grad, axis=0)))
```

```python
import math

import jax
import jax.numpy as jnp
from jax import lax
from jax.sharding import PartitionSpec as P

HEADS = 16
HEAD_DIM = 128
ROW_BLOCKS = 4


def owner_tables(owner_all, num_dev, tok_rows):
    owner_ids = jnp.arange(num_dev, dtype=jnp.int32)
    onehot = (owner_all[:, None] == owner_ids[None, :]).astype(jnp.int32)
    running = jnp.cumsum(onehot, axis=0) - onehot
    slot_index = jnp.sum(running * onehot, axis=1)
    per_shard = jnp.sum(onehot.reshape(num_dev, tok_rows, num_dev), axis=1)
    return (onehot, slot_index, per_shard)


def attend_both(head_rows, grad_heads, selected, bias_pair, row_count):
    length, _, per_dev, head_dim = head_rows.shape
    num_blocks, num_sel = selected.shape
    blk_rows = length // num_blocks
    score_scaling = 1.0 / math.sqrt(head_dim)

    def blocks(array):
        return array.reshape(num_blocks, blk_rows, per_dev, head_dim).transpose(2, 0, 1, 3)

    def unblock(array):
        return array.transpose(1, 2, 0, 3).reshape(length, per_dev * head_dim)

    query_tile_block = blocks(head_rows[:, 0])
    key_block = blocks(head_rows[:, 1])
    value_block = blocks(head_rows[:, 2])
    gradient_per_block = blocks(grad_heads)
    selected_keys = key_block[:, selected].reshape(
        per_dev, num_blocks, num_sel * blk_rows, head_dim
    )
    selected_values = value_block[:, selected].reshape(
        per_dev, num_blocks, num_sel * blk_rows, head_dim
    )
    col_kind = jnp.arange(num_sel * blk_rows) >= row_count * blk_rows
    key_offset_bias = jnp.where(col_kind[None, :], bias_pair[:, 1:2], bias_pair[:, 0:1])
    logit_scores = (
        jnp.einsum(
            "hbqd,hbkd->hbqk", query_tile_block, selected_keys, preferred_element_type=jnp.float32
        )
        * score_scaling
    )
    logit_scores = logit_scores + key_offset_bias[:, None, None, :]
    row_max = jnp.max(logit_scores, axis=-1, keepdims=True)
    exp_scores = jnp.exp(logit_scores - row_max)
    weights = exp_scores / jnp.sum(exp_scores, axis=-1, keepdims=True)
    reduced_weights = weights.astype(jnp.bfloat16)
    attention_result = jnp.einsum(
        "hbqk,hbkd->hbqd", reduced_weights, selected_values, preferred_element_type=jnp.float32
    ).astype(jnp.bfloat16)
    row_delta = jnp.sum(
        gradient_per_block.astype(jnp.float32) * attention_result.astype(jnp.float32),
        axis=-1,
        keepdims=True,
    )
    probability_gradient = jnp.einsum(
        "hbqd,hbkd->hbqk", gradient_per_block, selected_values, preferred_element_type=jnp.float32
    )
    dscore = weights * (probability_gradient - row_delta)
    bias_grad = jnp.stack(
        [
            jnp.sum(jnp.where(col_kind, 0.0, dscore), axis=(1, 2, 3)),
            jnp.sum(jnp.where(col_kind, dscore, 0.0), axis=(1, 2, 3)),
        ],
        axis=1,
    )
    score_gradient_reduced = dscore.astype(jnp.bfloat16)
    query_gradient = (
        jnp.einsum(
            "hbqk,hbkd->hbqd",
            score_gradient_reduced,
            selected_keys,
            preferred_element_type=jnp.float32,
        )
        * score_scaling
    )
    selected_key_gradient = (
        jnp.einsum(
            "hbqk,hbqd->hbkd",
            score_gradient_reduced,
            query_tile_block,
            preferred_element_type=jnp.float32,
        )
        * score_scaling
    )
    selected_value_gradient = jnp.einsum(
        "hbqk,hbqd->hbkd", reduced_weights, gradient_per_block, preferred_element_type=jnp.float32
    )
    block_hot = (
        selected[:, :, None] == jnp.arange(num_blocks, dtype=jnp.int32)[None, None, :]
    ).astype(jnp.float32)
    grad_key = jnp.einsum(
        "bjc,hbjtd->hctd",
        block_hot,
        selected_key_gradient.reshape(per_dev, num_blocks, num_sel, blk_rows, head_dim),
        precision=lax.Precision.HIGHEST,
    )
    grad_value = jnp.einsum(
        "bjc,hbjtd->hctd",
        block_hot,
        selected_value_gradient.reshape(per_dev, num_blocks, num_sel, blk_rows, head_dim),
        precision=lax.Precision.HIGHEST,
    )
    return (
        unblock(attention_result),
        unblock(query_gradient),
        unblock(grad_key),
        unblock(grad_value),
        bias_grad,
    )


def shards(qkv_owned, owner, band_rows, band_cols, bias, grad_out):
    num_dev = lax.axis_size("seq")
    my_index = lax.axis_index("seq")
    slot_count = qkv_owned.shape[1]
    features = qkv_owned.shape[2]
    tok_rows = grad_out.shape[1]
    row_width = grad_out.shape[2]
    per_dev = HEADS // num_dev
    group_width = per_dev * HEAD_DIM
    length = tok_rows * num_dev
    owner_all = owner[0]
    onehot, slot_index, _ = owner_tables(owner_all, num_dev, tok_rows)
    source = owner_all * slot_count + slot_index
    selected = jnp.concatenate([band_rows[0], band_cols[0]], axis=1)
    bias_pair = lax.dynamic_slice_in_dim(bias, my_index * per_dev, per_dev, 0)
    cell_rows = qkv_owned[0].reshape(slot_count, 3, num_dev, group_width)
    arrived = lax.all_to_all(cell_rows, "seq", split_axis=2, concat_axis=0, tiled=True)
    head_rows = jnp.take(arrived, source, axis=0).reshape(length, 3, per_dev, HEAD_DIM)
    grad_parts = grad_out[0].reshape(tok_rows, num_dev, group_width)
    grad_heads = lax.all_to_all(grad_parts, "seq", split_axis=1, concat_axis=0, tiled=True)
    grad_heads = grad_heads.reshape(length, per_dev, HEAD_DIM)
    attention_result, query_gradient, grad_key, grad_value, bias_grad = attend_both(
        head_rows, grad_heads, selected, bias_pair, ROW_BLOCKS
    )
    grad_rows = jnp.stack([query_gradient, grad_key, grad_value], axis=1).astype(jnp.bfloat16)
    send_back = (
        jnp.zeros((num_dev * slot_count, 3, group_width), jnp.bfloat16).at[source].set(grad_rows)
    )
    returned = lax.all_to_all(
        send_back.reshape(num_dev * slot_count, 3, 1, group_width),
        "seq",
        split_axis=0,
        concat_axis=2,
        tiled=True,
    )
    out_rows = lax.all_to_all(
        attention_result.reshape(length, 1, group_width),
        "seq",
        split_axis=0,
        concat_axis=1,
        tiled=True,
    )
    bias_total = lax.psum(bias_grad, "mp")
    return (
        out_rows.reshape(1, tok_rows, row_width),
        returned.reshape(1, slot_count, features),
        bias_total,
    )


def solution(mesh):
    in_specs = (
        P("mp", "seq", None),
        P("mp", None),
        P("mp", None, None),
        P("mp", None, None),
        P(),
        P("mp", "seq", None),
    )
    out_specs = (P("mp", "seq", None), P("mp", "seq", None), P("seq", None))
    return jax.shard_map(shards, mesh=mesh, in_specs=in_specs, out_specs=out_specs, check_vma=False)
```

```python
import math

import jax
import jax.numpy as jnp
from jax import lax
from jax.sharding import PartitionSpec as P

HEADS = 16
HEAD_DIM = 128
ROW_BLOCKS = 4


def owner_tables(owner_all, num_dev):
    owner_ids = jnp.arange(num_dev, dtype=jnp.int32)
    onehot = (owner_all[:, None] == owner_ids[None, :]).astype(jnp.int32)
    running = jnp.cumsum(onehot, axis=0) - onehot
    slot_index = jnp.sum(running * onehot, axis=1)
    named = jnp.sum(onehot, axis=0)
    return (slot_index, named)


def attend_head(query, key, value, grad, selected, bias_pair, row_count):
    length, head_dim = query.shape
    num_blocks, num_sel = selected.shape
    blk_rows = length // num_blocks
    score_scaling = 1.0 / math.sqrt(head_dim)

    def blocks(array):
        return array.reshape(num_blocks, blk_rows, head_dim)

    query_block = blocks(query)
    grad_block = blocks(grad)
    selected_keys = blocks(key)[selected].reshape(num_blocks, num_sel * blk_rows, head_dim)
    selected_values = blocks(value)[selected].reshape(num_blocks, num_sel * blk_rows, head_dim)
    col_kind = jnp.arange(num_sel * blk_rows) >= row_count * blk_rows
    key_offset_bias = jnp.where(col_kind, bias_pair[1], bias_pair[0])
    logit_scores = (
        jnp.einsum("bqd,bkd->bqk", query_block, selected_keys, preferred_element_type=jnp.float32)
        * score_scaling
    )
    logit_scores = logit_scores + key_offset_bias[None, None, :]
    row_max = jnp.max(logit_scores, axis=-1, keepdims=True)
    exp_scores = jnp.exp(logit_scores - row_max)
    weights = exp_scores / jnp.sum(exp_scores, axis=-1, keepdims=True)
    reduced_weights = weights.astype(jnp.bfloat16)
    attention_result = jnp.einsum(
        "bqk,bkd->bqd", reduced_weights, selected_values, preferred_element_type=jnp.float32
    ).astype(jnp.bfloat16)
    row_delta = jnp.sum(
        grad_block.astype(jnp.float32) * attention_result.astype(jnp.float32), axis=-1, keepdims=True
    )
    probability_gradient = jnp.einsum(
        "bqd,bkd->bqk", grad_block, selected_values, preferred_element_type=jnp.float32
    )
    dscore = weights * (probability_gradient - row_delta)
    bias_grad = jnp.stack(
        [jnp.sum(jnp.where(col_kind, 0.0, dscore)), jnp.sum(jnp.where(col_kind, dscore, 0.0))]
    )
    score_gradient_reduced = dscore.astype(jnp.bfloat16)
    query_gradient = (
        jnp.einsum(
            "bqk,bkd->bqd", score_gradient_reduced, selected_keys, preferred_element_type=jnp.float32
        )
        * score_scaling
    )
    selected_key_gradient = (
        jnp.einsum(
            "bqk,bqd->bkd", score_gradient_reduced, query_block, preferred_element_type=jnp.float32
        )
        * score_scaling
    )
    selected_value_gradient = jnp.einsum(
        "bqk,bqd->bkd", reduced_weights, grad_block, preferred_element_type=jnp.float32
    )
    block_hot = (
        selected[:, :, None] == jnp.arange(num_blocks, dtype=jnp.int32)[None, None, :]
    ).astype(jnp.float32)
    grad_key = jnp.einsum(
        "bjc,bjtd->ctd",
        block_hot,
        selected_key_gradient.reshape(num_blocks, num_sel, blk_rows, head_dim),
        precision=lax.Precision.HIGHEST,
    )
    grad_value = jnp.einsum(
        "bjc,bjtd->ctd",
        block_hot,
        selected_value_gradient.reshape(num_blocks, num_sel, blk_rows, head_dim),
        precision=lax.Precision.HIGHEST,
    )
    return (
        attention_result.reshape(length, head_dim),
        query_gradient.reshape(length, head_dim),
        grad_key.reshape(length, head_dim),
        grad_value.reshape(length, head_dim),
        bias_grad,
    )


def shards(qkv_owned, owner, band_rows, band_cols, bias, grad_out):
    num_dev = lax.axis_size("seq")
    my_index = lax.axis_index("seq")
    slot_count = qkv_owned.shape[1]
    features = qkv_owned.shape[2]
    tok_rows = grad_out.shape[1]
    row_width = grad_out.shape[2]
    per_dev = HEADS // num_dev
    group_width = per_dev * HEAD_DIM
    length = tok_rows * num_dev
    owner_all = owner[0]
    slot_index, named = owner_tables(owner_all, num_dev)
    source = owner_all * slot_count + slot_index
    named_before = jnp.cumsum(named) - named
    _, order = lax.sort((source, jnp.arange(length, dtype=jnp.int32)), num_keys=1)
    order_ext = jnp.concatenate([order, jnp.full((slot_count,), length, jnp.int32)])
    selected = jnp.concatenate([band_rows[0], band_cols[0]], axis=1)
    bias_pair = lax.dynamic_slice_in_dim(bias, my_index * per_dev, per_dev, 0)

    cell_rows = qkv_owned[0].reshape(slot_count, 3, num_dev, group_width).transpose(2, 1, 0, 3)
    arrived = lax.all_to_all(cell_rows, "seq", split_axis=0, concat_axis=0, tiled=True)
    grad_parts = grad_out[0].reshape(tok_rows, num_dev, group_width).transpose(1, 0, 2)
    grad_heads = lax.all_to_all(grad_parts, "seq", split_axis=0, concat_axis=0, tiled=True)
    grad_heads = grad_heads.reshape(length, group_width)
    parts = [arrived[owner_all, j, slot_index] for j in range(3)]

    results = []
    for h in range(per_dev):
        cols = slice(h * HEAD_DIM, (h + 1) * HEAD_DIM)
        results.append(
            attend_head(
                parts[0][:, cols],
                parts[1][:, cols],
                parts[2][:, cols],
                grad_heads[:, cols],
                selected,
                bias_pair[h],
                ROW_BLOCKS,
            )
        )
    attention_result = jnp.concatenate([r[0] for r in results], axis=1)
    grad_rows = jnp.stack(
        [jnp.concatenate([r[i] for r in results], axis=1) for i in (1, 2, 3)]
    ).astype(jnp.bfloat16)
    bias_grad = jnp.stack([r[4] for r in results])

    grad_rows = jnp.concatenate([grad_rows, jnp.zeros((3, 1, group_width), jnp.bfloat16)], axis=1)
    grad_sorted = jnp.take(grad_rows, order_ext, axis=1)
    within = jnp.arange(slot_count, dtype=jnp.int32)
    send_back = jnp.stack(
        [
            jnp.where(
                (within < named[o])[None, :, None],
                lax.dynamic_slice_in_dim(grad_sorted, named_before[o], slot_count, 1),
                jnp.zeros((), jnp.bfloat16),
            )
            for o in range(num_dev)
        ]
    )
    returned = lax.all_to_all(send_back, "seq", split_axis=0, concat_axis=0, tiled=True)
    grad_cells = returned.transpose(2, 1, 0, 3).reshape(slot_count, features)
    out_rows = lax.all_to_all(
        attention_result.reshape(num_dev, tok_rows, group_width),
        "seq",
        split_axis=0,
        concat_axis=0,
        tiled=True,
    )
    attended_rows = out_rows.transpose(1, 0, 2).reshape(tok_rows, row_width)
    bias_total = lax.psum(bias_grad, "mp")
    return (
        attended_rows.reshape(1, tok_rows, row_width),
        grad_cells.reshape(1, slot_count, features),
        bias_total,
    )


def solution(mesh):
    in_specs = (
        P("mp", "seq", None),
        P("mp", None),
        P("mp", None, None),
        P("mp", None, None),
        P(),
        P("mp", "seq", None),
    )
    out_specs = (P("mp", "seq", None), P("mp", "seq", None), P("seq", None))
    return jax.shard_map(shards, mesh=mesh, in_specs=in_specs, out_specs=out_specs, check_vma=False)
```

```python
import math

import jax
import jax.numpy as jnp
from jax import lax
from jax.experimental import pallas as pl
from jax.experimental.pallas import tpu as pltpu
from jax.sharding import PartitionSpec as P

INTERPRET = False

HEADS = 16
HEAD_DIM = 128
ROW_BLOCKS = 4


def owner_tables(owner_all, num_dev):
    owner_ids = jnp.arange(num_dev, dtype=jnp.int32)
    onehot = (owner_all[:, None] == owner_ids[None, :]).astype(jnp.int32)
    running = jnp.cumsum(onehot, axis=0) - onehot
    slot_index = jnp.sum(running * onehot, axis=1)
    return (slot_index, onehot)


def attend_head(query, key, value, grad, selected, bias_pair, row_count):
    length, head_dim = query.shape
    num_blocks, num_sel = selected.shape
    blk_rows = length // num_blocks
    score_scaling = 1.0 / math.sqrt(head_dim)

    def blocks(array):
        return array.reshape(num_blocks, blk_rows, head_dim)

    query_block = blocks(query)
    grad_block = blocks(grad)
    selected_keys = blocks(key)[selected].reshape(num_blocks, num_sel * blk_rows, head_dim)
    selected_values = blocks(value)[selected].reshape(num_blocks, num_sel * blk_rows, head_dim)
    col_kind = jnp.arange(num_sel * blk_rows) >= row_count * blk_rows
    key_offset_bias = jnp.where(col_kind, bias_pair[1], bias_pair[0])
    logit_scores = (
        jnp.einsum("bqd,bkd->bqk", query_block, selected_keys, preferred_element_type=jnp.float32)
        * score_scaling
    )
    logit_scores = logit_scores + key_offset_bias[None, None, :]
    row_max = jnp.max(logit_scores, axis=-1, keepdims=True)
    exp_scores = jnp.exp(logit_scores - row_max)
    weights = exp_scores / jnp.sum(exp_scores, axis=-1, keepdims=True)
    reduced_weights = weights.astype(jnp.bfloat16)
    attention_result = jnp.einsum(
        "bqk,bkd->bqd", reduced_weights, selected_values, preferred_element_type=jnp.float32
    ).astype(jnp.bfloat16)
    row_delta = jnp.sum(
        grad_block.astype(jnp.float32) * attention_result.astype(jnp.float32), axis=-1, keepdims=True
    )
    probability_gradient = jnp.einsum(
        "bqd,bkd->bqk", grad_block, selected_values, preferred_element_type=jnp.float32
    )
    dscore = weights * (probability_gradient - row_delta)
    bias_grad = jnp.stack(
        [jnp.sum(jnp.where(col_kind, 0.0, dscore)), jnp.sum(jnp.where(col_kind, dscore, 0.0))]
    )
    score_gradient_reduced = dscore.astype(jnp.bfloat16)
    query_gradient = (
        jnp.einsum(
            "bqk,bkd->bqd", score_gradient_reduced, selected_keys, preferred_element_type=jnp.float32
        )
        * score_scaling
    )
    selected_key_gradient = (
        jnp.einsum(
            "bqk,bqd->bkd", score_gradient_reduced, query_block, preferred_element_type=jnp.float32
        )
        * score_scaling
    )
    selected_value_gradient = jnp.einsum(
        "bqk,bqd->bkd", reduced_weights, grad_block, preferred_element_type=jnp.float32
    )
    block_hot = (
        selected[:, :, None] == jnp.arange(num_blocks, dtype=jnp.int32)[None, None, :]
    ).astype(jnp.float32)
    grad_key = jnp.einsum(
        "bjc,bjtd->ctd",
        block_hot,
        selected_key_gradient.reshape(num_blocks, num_sel, blk_rows, head_dim),
        precision=lax.Precision.HIGHEST,
    )
    grad_value = jnp.einsum(
        "bjc,bjtd->ctd",
        block_hot,
        selected_value_gradient.reshape(num_blocks, num_sel, blk_rows, head_dim),
        precision=lax.Precision.HIGHEST,
    )
    return (
        attention_result.reshape(length, head_dim),
        query_gradient.reshape(length, head_dim),
        grad_key.reshape(length, head_dim),
        grad_value.reshape(length, head_dim),
        bias_grad,
    )


def split_heads(cells, num_dev, group_width):
    slot_count, features = cells.shape
    span = num_dev * group_width

    def body(x_ref, o_ref):
        for h in range(num_dev):
            o_ref[h, 0] = x_ref[:, h * group_width:(h + 1) * group_width]

    return pl.pallas_call(
        body,
        grid=(features // span,),
        in_specs=[pl.BlockSpec((slot_count, span), lambda j: (0, j))],
        out_specs=pl.BlockSpec((num_dev, 1, slot_count, group_width), lambda j: (0, j, 0, 0)),
        out_shape=jax.ShapeDtypeStruct((num_dev, features // span, slot_count, group_width), cells.dtype),
        interpret=INTERPRET,
    )(cells)


def join_heads(parts):
    num_dev, kinds, slot_count, group_width = parts.shape
    span = num_dev * group_width

    def body(x_ref, o_ref):
        for h in range(num_dev):
            o_ref[:, h * group_width:(h + 1) * group_width] = x_ref[h, 0]

    return pl.pallas_call(
        body,
        grid=(kinds,),
        in_specs=[pl.BlockSpec((num_dev, 1, slot_count, group_width), lambda j: (0, j, 0, 0))],
        out_specs=pl.BlockSpec((slot_count, span), lambda j: (0, j)),
        out_shape=jax.ShapeDtypeStruct((slot_count, kinds * span), parts.dtype),
        interpret=INTERPRET,
    )(parts)


def shards(qkv_owned, owner, band_rows, band_cols, bias, grad_out):
    num_dev = lax.axis_size("seq")
    my_index = lax.axis_index("seq")
    slot_count = qkv_owned.shape[1]
    features = qkv_owned.shape[2]
    tok_rows = grad_out.shape[1]
    row_width = grad_out.shape[2]
    per_dev = HEADS // num_dev
    group_width = per_dev * HEAD_DIM
    length = tok_rows * num_dev
    owner_all = owner[0]
    slot_index, _ = owner_tables(owner_all, num_dev)
    source = owner_all * slot_count + slot_index
    pick = (source[:, None] == jnp.arange(num_dev * slot_count, dtype=jnp.int32)[None, :]).astype(
        jnp.bfloat16
    ).reshape(length, num_dev, slot_count)
    selected = jnp.concatenate([band_rows[0], band_cols[0]], axis=1)
    bias_pair = lax.dynamic_slice_in_dim(bias, my_index * per_dev, per_dev, 0)

    cell_rows = split_heads(qkv_owned[0], num_dev, group_width)
    arrived = lax.all_to_all(cell_rows, "seq", split_axis=0, concat_axis=0, tiled=True)
    grad_parts = grad_out[0].reshape(tok_rows, num_dev, group_width).transpose(1, 0, 2)
    grad_heads = lax.all_to_all(grad_parts, "seq", split_axis=0, concat_axis=0, tiled=True)
    grad_heads = grad_heads.reshape(length, group_width)
    parts = jnp.einsum(
        "pos,ojsd->jpd", pick, arrived, preferred_element_type=jnp.float32
    ).astype(jnp.bfloat16)

    results = []
    for h in range(per_dev):
        cols = slice(h * HEAD_DIM, (h + 1) * HEAD_DIM)
        results.append(
            attend_head(
                parts[0][:, cols],
                parts[1][:, cols],
                parts[2][:, cols],
                grad_heads[:, cols],
                selected,
                bias_pair[h],
                ROW_BLOCKS,
            )
        )
    attention_result = jnp.concatenate([r[0] for r in results], axis=1)
    grad_rows = jnp.stack(
        [jnp.concatenate([r[i] for r in results], axis=1) for i in (1, 2, 3)]
    ).astype(jnp.bfloat16)
    bias_grad = jnp.stack([r[4] for r in results])

    send_back = jnp.einsum(
        "pos,jpd->ojsd", pick, grad_rows, preferred_element_type=jnp.float32
    ).astype(jnp.bfloat16)
    returned = lax.all_to_all(send_back, "seq", split_axis=0, concat_axis=0, tiled=True)
    grad_cells = join_heads(returned)
    out_rows = lax.all_to_all(
        attention_result.reshape(num_dev, tok_rows, group_width),
        "seq",
        split_axis=0,
        concat_axis=0,
        tiled=True,
    )
    attended_rows = out_rows.transpose(1, 0, 2).reshape(tok_rows, row_width)
    bias_total = lax.psum(bias_grad, "mp")
    return (
        attended_rows.reshape(1, tok_rows, row_width),
        grad_cells.reshape(1, slot_count, features),
        bias_total,
    )


def solution(mesh):
    in_specs = (
        P("mp", "seq", None),
        P("mp", None),
        P("mp", None, None),
        P("mp", None, None),
        P(),
        P("mp", "seq", None),
    )
    out_specs = (P("mp", "seq", None), P("mp", "seq", None), P("seq", None))
    return jax.shard_map(shards, mesh=mesh, in_specs=in_specs, out_specs=out_specs, check_vma=False)
```

```python
import functools
import math

import jax
import jax.numpy as jnp
from jax import lax
from jax.experimental import pallas as pl
from jax.experimental.pallas import tpu as pltpu
from jax.sharding import PartitionSpec as P

INTERPRET = False

HEADS = 16
HEAD_DIM = 128
ROW_BLOCKS = 4


def owner_tables(owner_all, num_dev):
    owner_ids = jnp.arange(num_dev, dtype=jnp.int32)
    onehot = (owner_all[:, None] == owner_ids[None, :]).astype(jnp.int32)
    running = jnp.cumsum(onehot, axis=0) - onehot
    slot_index = jnp.sum(running * onehot, axis=1)
    return (slot_index, onehot)


def attend_head(query, key, value, grad, selected, bias_pair, row_count):
    length, head_dim = query.shape
    num_blocks, num_sel = selected.shape
    blk_rows = length // num_blocks
    score_scaling = 1.0 / math.sqrt(head_dim)

    def blocks(array):
        return array.reshape(num_blocks, blk_rows, head_dim)

    query_block = blocks(query)
    grad_block = blocks(grad)
    selected_keys = blocks(key)[selected].reshape(num_blocks, num_sel * blk_rows, head_dim)
    selected_values = blocks(value)[selected].reshape(num_blocks, num_sel * blk_rows, head_dim)
    col_kind = jnp.arange(num_sel * blk_rows) >= row_count * blk_rows
    key_offset_bias = jnp.where(col_kind, bias_pair[1], bias_pair[0])
    logit_scores = (
        jnp.einsum("bqd,bkd->bqk", query_block, selected_keys, preferred_element_type=jnp.float32)
        * score_scaling
    )
    logit_scores = logit_scores + key_offset_bias[None, None, :]
    row_max = jnp.max(logit_scores, axis=-1, keepdims=True)
    exp_scores = jnp.exp(logit_scores - row_max)
    weights = exp_scores / jnp.sum(exp_scores, axis=-1, keepdims=True)
    reduced_weights = weights.astype(jnp.bfloat16)
    attention_result = jnp.einsum(
        "bqk,bkd->bqd", reduced_weights, selected_values, preferred_element_type=jnp.float32
    ).astype(jnp.bfloat16)
    row_delta = jnp.sum(
        grad_block.astype(jnp.float32) * attention_result.astype(jnp.float32), axis=-1, keepdims=True
    )
    probability_gradient = jnp.einsum(
        "bqd,bkd->bqk", grad_block, selected_values, preferred_element_type=jnp.float32
    )
    dscore = weights * (probability_gradient - row_delta)
    bias_grad = jnp.stack(
        [jnp.sum(jnp.where(col_kind, 0.0, dscore)), jnp.sum(jnp.where(col_kind, dscore, 0.0))]
    )
    score_gradient_reduced = dscore.astype(jnp.bfloat16)
    query_gradient = (
        jnp.einsum(
            "bqk,bkd->bqd", score_gradient_reduced, selected_keys, preferred_element_type=jnp.float32
        )
        * score_scaling
    )
    selected_key_gradient = (
        jnp.einsum(
            "bqk,bqd->bkd", score_gradient_reduced, query_block, preferred_element_type=jnp.float32
        )
        * score_scaling
    )
    selected_value_gradient = jnp.einsum(
        "bqk,bqd->bkd", reduced_weights, grad_block, preferred_element_type=jnp.float32
    )
    block_hot = (
        selected[:, :, None] == jnp.arange(num_blocks, dtype=jnp.int32)[None, None, :]
    ).astype(jnp.float32)
    grad_key = jnp.einsum(
        "bjc,bjtd->ctd",
        block_hot,
        selected_key_gradient.reshape(num_blocks, num_sel, blk_rows, head_dim),
        precision=lax.Precision.HIGHEST,
    )
    grad_value = jnp.einsum(
        "bjc,bjtd->ctd",
        block_hot,
        selected_value_gradient.reshape(num_blocks, num_sel, blk_rows, head_dim),
        precision=lax.Precision.HIGHEST,
    )
    return (
        attention_result.reshape(length, head_dim),
        query_gradient.reshape(length, head_dim),
        grad_key.reshape(length, head_dim),
        grad_value.reshape(length, head_dim),
        bias_grad,
    )


def attention_kernel(row_count, sel_ref, bias_ref, qkv_ref, g_ref, o_ref, grads_ref, db_ref, dk_acc, dv_acc):
    num_blocks, num_sel = sel_ref.shape
    head_dim = g_ref.shape[1]
    blk = g_ref.shape[0] // num_blocks
    score_scaling = 1.0 / math.sqrt(head_dim)
    dk_acc[...] = jnp.zeros_like(dk_acc)
    dv_acc[...] = jnp.zeros_like(dv_acc)
    col_kind = lax.broadcasted_iota(jnp.int32, (blk, num_sel * blk), 1) >= row_count * blk
    key_offset_bias = jnp.where(col_kind, bias_ref[1], bias_ref[0])
    trans_a = (((0,), (0,)), ((), ()))
    trans_b = (((1,), (1,)), ((), ()))

    def body(b, carry):
        acc_row, acc_col = carry
        start = pl.multiple_of(b * blk, blk)
        query_block = qkv_ref[0, pl.ds(start, blk), :]
        grad_block = g_ref[pl.ds(start, blk), :]
        picks = [pl.multiple_of(sel_ref[b, i] * blk, blk) for i in range(num_sel)]
        keys = jnp.concatenate([qkv_ref[1, pl.ds(p, blk), :] for p in picks], axis=0)
        values = jnp.concatenate([qkv_ref[2, pl.ds(p, blk), :] for p in picks], axis=0)
        logits = lax.dot_general(query_block, keys, trans_b, preferred_element_type=jnp.float32)
        logits = logits * score_scaling + key_offset_bias
        row_max = jnp.max(logits, axis=1, keepdims=True)
        exp_scores = jnp.exp(logits - row_max)
        weights = exp_scores / jnp.sum(exp_scores, axis=1, keepdims=True)
        reduced_weights = weights.astype(jnp.bfloat16)
        result = jnp.dot(reduced_weights, values, preferred_element_type=jnp.float32).astype(jnp.bfloat16)
        o_ref[pl.ds(start, blk), :] = result
        row_delta = jnp.sum(
            grad_block.astype(jnp.float32) * result.astype(jnp.float32), axis=1, keepdims=True
        )
        prob_grad = lax.dot_general(grad_block, values, trans_b, preferred_element_type=jnp.float32)
        dscore = weights * (prob_grad - row_delta)
        acc_row = acc_row + jnp.sum(jnp.where(col_kind, 0.0, dscore), keepdims=True)
        acc_col = acc_col + jnp.sum(jnp.where(col_kind, dscore, 0.0), keepdims=True)
        reduced_dscore = dscore.astype(jnp.bfloat16)
        query_grad = jnp.dot(reduced_dscore, keys, preferred_element_type=jnp.float32) * score_scaling
        grads_ref[0, pl.ds(start, blk), :] = query_grad.astype(grads_ref.dtype)
        key_grad = lax.dot_general(
            reduced_dscore, query_block, trans_a, preferred_element_type=jnp.float32
        ) * score_scaling
        value_grad = lax.dot_general(
            reduced_weights, grad_block, trans_a, preferred_element_type=jnp.float32
        )
        for i, p in enumerate(picks):
            rows = pl.ds(p, blk)
            dk_acc[rows, :] += key_grad[i * blk:(i + 1) * blk]
            dv_acc[rows, :] += value_grad[i * blk:(i + 1) * blk]
        return acc_row, acc_col

    zero = jnp.zeros((1, 1), jnp.float32)
    acc_row, acc_col = lax.fori_loop(0, num_blocks, body, (zero, zero))
    grads_ref[1] = dk_acc[...].astype(grads_ref.dtype)
    grads_ref[2] = dv_acc[...].astype(grads_ref.dtype)
    lane = lax.broadcasted_iota(jnp.int32, db_ref.shape, 1)
    db_ref[...] = jnp.where(lane == 0, acc_row, jnp.where(lane == 1, acc_col, 0.0))


def attend_fused(parts, grad, selected, bias_pair, row_count):
    _, length, head_dim = parts.shape
    smem = pl.BlockSpec(memory_space=pltpu.SMEM)
    vmem = pl.BlockSpec(memory_space=pltpu.VMEM)
    flops = 6 * 2 * length * selected.shape[1] * (length // selected.shape[0]) * head_dim
    result, grads, bias_grad = pl.pallas_call(
        functools.partial(attention_kernel, row_count),
        in_specs=[smem, smem, vmem, vmem],
        out_specs=[vmem, vmem, vmem],
        out_shape=[
            jax.ShapeDtypeStruct((length, head_dim), jnp.bfloat16),
            jax.ShapeDtypeStruct((3, length, head_dim), jnp.bfloat16),
            jax.ShapeDtypeStruct((1, 128), jnp.float32),
        ],
        scratch_shapes=[
            pltpu.VMEM((length, head_dim), jnp.float32),
            pltpu.VMEM((length, head_dim), jnp.float32),
        ],
        cost_estimate=pl.CostEstimate(
            flops=flops, transcendentals=length * selected.shape[1] * 128, bytes_accessed=12 * length * head_dim
        ),
        interpret=INTERPRET,
    )(selected, bias_pair, parts, grad)
    return result, grads, bias_grad[0, :2]


def split_heads(cells, num_dev, group_width):
    slot_count, features = cells.shape
    span = num_dev * group_width

    def body(x_ref, o_ref):
        for h in range(num_dev):
            o_ref[h, 0] = x_ref[:, h * group_width:(h + 1) * group_width]

    return pl.pallas_call(
        body,
        grid=(features // span,),
        in_specs=[pl.BlockSpec((slot_count, span), lambda j: (0, j))],
        out_specs=pl.BlockSpec((num_dev, 1, slot_count, group_width), lambda j: (0, j, 0, 0)),
        out_shape=jax.ShapeDtypeStruct((num_dev, features // span, slot_count, group_width), cells.dtype),
        interpret=INTERPRET,
    )(cells)


def join_heads(parts):
    num_dev, kinds, slot_count, group_width = parts.shape
    span = num_dev * group_width

    def body(x_ref, o_ref):
        for h in range(num_dev):
            o_ref[:, h * group_width:(h + 1) * group_width] = x_ref[h, 0]

    return pl.pallas_call(
        body,
        grid=(kinds,),
        in_specs=[pl.BlockSpec((num_dev, 1, slot_count, group_width), lambda j: (0, j, 0, 0))],
        out_specs=pl.BlockSpec((slot_count, span), lambda j: (0, j)),
        out_shape=jax.ShapeDtypeStruct((slot_count, kinds * span), parts.dtype),
        interpret=INTERPRET,
    )(parts)


def shards(qkv_owned, owner, band_rows, band_cols, bias, grad_out):
    num_dev = lax.axis_size("seq")
    my_index = lax.axis_index("seq")
    slot_count = qkv_owned.shape[1]
    features = qkv_owned.shape[2]
    tok_rows = grad_out.shape[1]
    row_width = grad_out.shape[2]
    per_dev = HEADS // num_dev
    group_width = per_dev * HEAD_DIM
    length = tok_rows * num_dev
    owner_all = owner[0]
    slot_index, _ = owner_tables(owner_all, num_dev)
    source = owner_all * slot_count + slot_index
    pick = (source[:, None] == jnp.arange(num_dev * slot_count, dtype=jnp.int32)[None, :]).astype(
        jnp.bfloat16
    ).reshape(length, num_dev, slot_count)
    selected = jnp.concatenate([band_rows[0], band_cols[0]], axis=1)
    bias_pair = lax.dynamic_slice_in_dim(bias, my_index * per_dev, per_dev, 0)

    cell_rows = split_heads(qkv_owned[0], num_dev, group_width)
    arrived = lax.all_to_all(cell_rows, "seq", split_axis=0, concat_axis=0, tiled=True)
    grad_parts = grad_out[0].reshape(tok_rows, num_dev, group_width).transpose(1, 0, 2)
    grad_heads = lax.all_to_all(grad_parts, "seq", split_axis=0, concat_axis=0, tiled=True)
    grad_heads = grad_heads.reshape(length, group_width)
    parts = jnp.einsum(
        "pos,ojsd->jpd", pick, arrived, preferred_element_type=jnp.float32
    ).astype(jnp.bfloat16)

    attention_result, grad_rows, bias_grad = attend_fused(
        parts, grad_heads, selected, bias_pair[0], ROW_BLOCKS
    )
    bias_grad = bias_grad[None, :]

    send_back = jnp.einsum(
        "pos,jpd->ojsd", pick, grad_rows, preferred_element_type=jnp.float32
    ).astype(jnp.bfloat16)
    returned = lax.all_to_all(send_back, "seq", split_axis=0, concat_axis=0, tiled=True)
    grad_cells = join_heads(returned)
    out_rows = lax.all_to_all(
        attention_result.reshape(num_dev, tok_rows, group_width),
        "seq",
        split_axis=0,
        concat_axis=0,
        tiled=True,
    )
    attended_rows = out_rows.transpose(1, 0, 2).reshape(tok_rows, row_width)
    bias_total = lax.psum(bias_grad, "mp")
    return (
        attended_rows.reshape(1, tok_rows, row_width),
        grad_cells.reshape(1, slot_count, features),
        bias_total,
    )


def solution(mesh):
    in_specs = (
        P("mp", "seq", None),
        P("mp", None),
        P("mp", None, None),
        P("mp", None, None),
        P(),
        P("mp", "seq", None),
    )
    out_specs = (P("mp", "seq", None), P("mp", "seq", None), P("seq", None))
    return jax.shard_map(shards, mesh=mesh, in_specs=in_specs, out_specs=out_specs, check_vma=False)
```

```python
import functools
import math

import jax
import jax.numpy as jnp
from jax import lax
from jax.experimental import pallas as pl
from jax.experimental.pallas import tpu as pltpu
from jax.sharding import PartitionSpec as P

INTERPRET = False

HEADS = 16
HEAD_DIM = 128
ROW_BLOCKS = 4


def owner_tables(owner_all, num_dev):
    owner_ids = jnp.arange(num_dev, dtype=jnp.int32)
    onehot = (owner_all[:, None] == owner_ids[None, :]).astype(jnp.int32)
    running = jnp.cumsum(onehot, axis=0) - onehot
    slot_index = jnp.sum(running * onehot, axis=1)
    return (slot_index, onehot)


def attend_head(query, key, value, grad, selected, bias_pair, row_count):
    length, head_dim = query.shape
    num_blocks, num_sel = selected.shape
    blk_rows = length // num_blocks
    score_scaling = 1.0 / math.sqrt(head_dim)

    def blocks(array):
        return array.reshape(num_blocks, blk_rows, head_dim)

    query_block = blocks(query)
    grad_block = blocks(grad)
    selected_keys = blocks(key)[selected].reshape(num_blocks, num_sel * blk_rows, head_dim)
    selected_values = blocks(value)[selected].reshape(num_blocks, num_sel * blk_rows, head_dim)
    col_kind = jnp.arange(num_sel * blk_rows) >= row_count * blk_rows
    key_offset_bias = jnp.where(col_kind, bias_pair[1], bias_pair[0])
    logit_scores = (
        jnp.einsum("bqd,bkd->bqk", query_block, selected_keys, preferred_element_type=jnp.float32)
        * score_scaling
    )
    logit_scores = logit_scores + key_offset_bias[None, None, :]
    row_max = jnp.max(logit_scores, axis=-1, keepdims=True)
    exp_scores = jnp.exp(logit_scores - row_max)
    weights = exp_scores / jnp.sum(exp_scores, axis=-1, keepdims=True)
    reduced_weights = weights.astype(jnp.bfloat16)
    attention_result = jnp.einsum(
        "bqk,bkd->bqd", reduced_weights, selected_values, preferred_element_type=jnp.float32
    ).astype(jnp.bfloat16)
    row_delta = jnp.sum(
        grad_block.astype(jnp.float32) * attention_result.astype(jnp.float32), axis=-1, keepdims=True
    )
    probability_gradient = jnp.einsum(
        "bqd,bkd->bqk", grad_block, selected_values, preferred_element_type=jnp.float32
    )
    dscore = weights * (probability_gradient - row_delta)
    bias_grad = jnp.stack(
        [jnp.sum(jnp.where(col_kind, 0.0, dscore)), jnp.sum(jnp.where(col_kind, dscore, 0.0))]
    )
    score_gradient_reduced = dscore.astype(jnp.bfloat16)
    query_gradient = (
        jnp.einsum(
            "bqk,bkd->bqd", score_gradient_reduced, selected_keys, preferred_element_type=jnp.float32
        )
        * score_scaling
    )
    selected_key_gradient = (
        jnp.einsum(
            "bqk,bqd->bkd", score_gradient_reduced, query_block, preferred_element_type=jnp.float32
        )
        * score_scaling
    )
    selected_value_gradient = jnp.einsum(
        "bqk,bqd->bkd", reduced_weights, grad_block, preferred_element_type=jnp.float32
    )
    block_hot = (
        selected[:, :, None] == jnp.arange(num_blocks, dtype=jnp.int32)[None, None, :]
    ).astype(jnp.float32)
    grad_key = jnp.einsum(
        "bjc,bjtd->ctd",
        block_hot,
        selected_key_gradient.reshape(num_blocks, num_sel, blk_rows, head_dim),
        precision=lax.Precision.HIGHEST,
    )
    grad_value = jnp.einsum(
        "bjc,bjtd->ctd",
        block_hot,
        selected_value_gradient.reshape(num_blocks, num_sel, blk_rows, head_dim),
        precision=lax.Precision.HIGHEST,
    )
    return (
        attention_result.reshape(length, head_dim),
        query_gradient.reshape(length, head_dim),
        grad_key.reshape(length, head_dim),
        grad_value.reshape(length, head_dim),
        bias_grad,
    )


def attention_kernel(row_count, sel_ref, bias_ref, qkv_ref, g_ref, o_ref, grads_ref, db_ref, dk_acc, dv_acc):
    num_blocks, num_sel = sel_ref.shape
    head_dim = g_ref.shape[1]
    blk = g_ref.shape[0] // num_blocks
    score_scaling = 1.0 / math.sqrt(head_dim)
    dk_acc[...] = jnp.zeros_like(dk_acc)
    dv_acc[...] = jnp.zeros_like(dv_acc)
    col_kind = lax.broadcasted_iota(jnp.int32, (blk, num_sel * blk), 1) >= row_count * blk
    key_offset_bias = jnp.where(col_kind, bias_ref[1], bias_ref[0])
    trans_a = (((0,), (0,)), ((), ()))
    trans_b = (((1,), (1,)), ((), ()))

    def body(b, carry):
        acc_row, acc_col = carry
        start = pl.multiple_of(b * blk, blk)
        query_block = qkv_ref[0, pl.ds(start, blk), :]
        grad_block = g_ref[pl.ds(start, blk), :]
        picks = [pl.multiple_of(sel_ref[b, i] * blk, blk) for i in range(num_sel)]
        keys = jnp.concatenate([qkv_ref[1, pl.ds(p, blk), :] for p in picks], axis=0)
        values = jnp.concatenate([qkv_ref[2, pl.ds(p, blk), :] for p in picks], axis=0)
        logits = lax.dot_general(query_block, keys, trans_b, preferred_element_type=jnp.float32)
        logits = logits * score_scaling + key_offset_bias
        row_max = jnp.max(logits, axis=1, keepdims=True)
        exp_scores = jnp.exp(logits - row_max)
        weights = exp_scores / jnp.sum(exp_scores, axis=1, keepdims=True)
        reduced_weights = weights.astype(jnp.bfloat16)
        result = jnp.dot(reduced_weights, values, preferred_element_type=jnp.float32).astype(jnp.bfloat16)
        o_ref[pl.ds(start, blk), :] = result
        row_delta = jnp.sum(
            grad_block.astype(jnp.float32) * result.astype(jnp.float32), axis=1, keepdims=True
        )
        prob_grad = lax.dot_general(grad_block, values, trans_b, preferred_element_type=jnp.float32)
        dscore = weights * (prob_grad - row_delta)
        acc_row = acc_row + jnp.sum(jnp.where(col_kind, 0.0, dscore), keepdims=True)
        acc_col = acc_col + jnp.sum(jnp.where(col_kind, dscore, 0.0), keepdims=True)
        reduced_dscore = dscore.astype(jnp.bfloat16)
        query_grad = jnp.dot(reduced_dscore, keys, preferred_element_type=jnp.float32) * score_scaling
        grads_ref[0, pl.ds(start, blk), :] = query_grad.astype(grads_ref.dtype)
        key_grad = lax.dot_general(
            reduced_dscore, query_block, trans_a, preferred_element_type=jnp.float32
        ) * score_scaling
        value_grad = lax.dot_general(
            reduced_weights, grad_block, trans_a, preferred_element_type=jnp.float32
        )
        for i, p in enumerate(picks):
            rows = pl.ds(p, blk)
            dk_acc[rows, :] += key_grad[i * blk:(i + 1) * blk]
            dv_acc[rows, :] += value_grad[i * blk:(i + 1) * blk]
        return acc_row, acc_col

    zero = jnp.zeros((1, 1), jnp.float32)
    acc_row, acc_col = lax.fori_loop(0, num_blocks, body, (zero, zero))
    grads_ref[1] = dk_acc[...].astype(grads_ref.dtype)
    grads_ref[2] = dv_acc[...].astype(grads_ref.dtype)
    lane = lax.broadcasted_iota(jnp.int32, db_ref.shape, 1)
    db_ref[...] = jnp.where(lane == 0, acc_row, jnp.where(lane == 1, acc_col, 0.0))


def attend_fused(parts, grad, selected, bias_pair, row_count):
    _, length, head_dim = parts.shape
    smem = pl.BlockSpec(memory_space=pltpu.SMEM)
    vmem = pl.BlockSpec(memory_space=pltpu.VMEM)
    flops = 6 * 2 * length * selected.shape[1] * (length // selected.shape[0]) * head_dim
    result, grads, bias_grad = pl.pallas_call(
        functools.partial(attention_kernel, row_count),
        in_specs=[smem, smem, vmem, vmem],
        out_specs=[vmem, vmem, vmem],
        out_shape=[
            jax.ShapeDtypeStruct((length, head_dim), jnp.bfloat16),
            jax.ShapeDtypeStruct((3, length, head_dim), jnp.bfloat16),
            jax.ShapeDtypeStruct((1, 128), jnp.float32),
        ],
        scratch_shapes=[
            pltpu.VMEM((length, head_dim), jnp.float32),
            pltpu.VMEM((length, head_dim), jnp.float32),
        ],
        cost_estimate=pl.CostEstimate(
            flops=flops, transcendentals=length * selected.shape[1] * 128, bytes_accessed=12 * length * head_dim
        ),
        interpret=INTERPRET,
    )(selected, bias_pair, parts, grad)
    return result, grads, bias_grad[0, :2]


WINDOW = 48
ALIGN = 16


def gather_kernel(starts_ref, cols_ref, cells_ref, o_ref):
    q = pl.program_id(0)
    num_dev, kinds, _, _ = cells_ref.shape
    blk = cols_ref.shape[0]
    picker = (
        lax.broadcasted_iota(jnp.int32, (blk, num_dev * WINDOW), 1) == cols_ref[...]
    ).astype(cells_ref.dtype)
    for j in range(kinds):
        window = jnp.concatenate(
            [
                cells_ref[o, j, pl.ds(pl.multiple_of(starts_ref[q, o], ALIGN), WINDOW), :]
                for o in range(num_dev)
            ],
            axis=0,
        )
        o_ref[j] = jnp.dot(picker, window, preferred_element_type=jnp.float32).astype(o_ref.dtype)


def gather_rows(cells, starts, cols):
    num_dev, kinds, slot_count, width = cells.shape
    length = cols.shape[0]
    blk = length // num_dev
    return pl.pallas_call(
        gather_kernel,
        grid_spec=pltpu.PrefetchScalarGridSpec(
            num_scalar_prefetch=1,
            grid=(num_dev,),
            in_specs=[
                pl.BlockSpec((blk, 1), lambda q, s: (q, 0)),
                pl.BlockSpec((num_dev, kinds, slot_count, width), lambda q, s: (0, 0, 0, 0)),
            ],
            out_specs=pl.BlockSpec((kinds, blk, width), lambda q, s: (0, q, 0)),
        ),
        out_shape=jax.ShapeDtypeStruct((kinds, length, width), cells.dtype),
        cost_estimate=pl.CostEstimate(
            flops=2 * kinds * length * num_dev * WINDOW * width,
            transcendentals=0,
            bytes_accessed=2 * (cells.size + kinds * length * width),
        ),
        interpret=INTERPRET,
    )(starts, cols.reshape(length, 1), cells)


def scatter_kernel(starts_ref, cols_ref, grads_ref, o_ref, acc):
    num_dev = starts_ref.shape[0]
    kinds, length, width = grads_ref.shape
    blk = length // num_dev
    acc[...] = jnp.zeros_like(acc)

    def body(q, carry):
        spread = (
            lax.broadcasted_iota(jnp.int32, (num_dev * WINDOW, blk), 0) == cols_ref[pl.ds(q, 1), :]
        ).astype(grads_ref.dtype)
        begin = pl.multiple_of(q * blk, blk)
        for j in range(kinds):
            placed = jnp.dot(spread, grads_ref[j, pl.ds(begin, blk), :], preferred_element_type=jnp.float32)
            for o in range(num_dev):
                rows = pl.ds(pl.multiple_of(starts_ref[q, o], ALIGN), WINDOW)
                acc[o, j, rows, :] += placed[o * WINDOW:(o + 1) * WINDOW]
        return carry

    lax.fori_loop(0, num_dev, body, 0)
    o_ref[...] = acc[...].astype(o_ref.dtype)


def scatter_rows(grads, starts, cols, slot_count):
    kinds, length, width = grads.shape
    num_dev = starts.shape[0]
    smem = pl.BlockSpec(memory_space=pltpu.SMEM)
    vmem = pl.BlockSpec(memory_space=pltpu.VMEM)
    return pl.pallas_call(
        scatter_kernel,
        in_specs=[smem, vmem, vmem],
        out_specs=vmem,
        out_shape=jax.ShapeDtypeStruct((num_dev, kinds, slot_count, width), grads.dtype),
        scratch_shapes=[pltpu.VMEM((num_dev, kinds, slot_count, width), jnp.float32)],
        cost_estimate=pl.CostEstimate(
            flops=2 * kinds * length * num_dev * WINDOW * width,
            transcendentals=0,
            bytes_accessed=2 * (grads.size + num_dev * kinds * slot_count * width),
        ),
        interpret=INTERPRET,
    )(starts, cols.reshape(num_dev, length // num_dev), grads)


def split_heads(cells, num_dev, group_width):
    slot_count, features = cells.shape
    span = num_dev * group_width

    def body(x_ref, o_ref):
        for h in range(num_dev):
            o_ref[h, 0] = x_ref[:, h * group_width:(h + 1) * group_width]

    return pl.pallas_call(
        body,
        grid=(features // span,),
        in_specs=[pl.BlockSpec((slot_count, span), lambda j: (0, j))],
        out_specs=pl.BlockSpec((num_dev, 1, slot_count, group_width), lambda j: (0, j, 0, 0)),
        out_shape=jax.ShapeDtypeStruct((num_dev, features // span, slot_count, group_width), cells.dtype),
        interpret=INTERPRET,
    )(cells)


def join_heads(parts):
    num_dev, kinds, slot_count, group_width = parts.shape
    span = num_dev * group_width

    def body(x_ref, o_ref):
        for h in range(num_dev):
            o_ref[:, h * group_width:(h + 1) * group_width] = x_ref[h, 0]

    return pl.pallas_call(
        body,
        grid=(kinds,),
        in_specs=[pl.BlockSpec((num_dev, 1, slot_count, group_width), lambda j: (0, j, 0, 0))],
        out_specs=pl.BlockSpec((slot_count, span), lambda j: (0, j)),
        out_shape=jax.ShapeDtypeStruct((slot_count, kinds * span), parts.dtype),
        interpret=INTERPRET,
    )(parts)


def shards(qkv_owned, owner, band_rows, band_cols, bias, grad_out):
    num_dev = lax.axis_size("seq")
    my_index = lax.axis_index("seq")
    slot_count = qkv_owned.shape[1]
    features = qkv_owned.shape[2]
    tok_rows = grad_out.shape[1]
    row_width = grad_out.shape[2]
    per_dev = HEADS // num_dev
    group_width = per_dev * HEAD_DIM
    length = tok_rows * num_dev
    owner_all = owner[0]
    slot_index, onehot = owner_tables(owner_all, num_dev)
    shard_hot = onehot.reshape(num_dev, tok_rows, num_dev)
    per_shard = jnp.sum(shard_hot, axis=1)
    before = jnp.cumsum(per_shard, axis=0) - per_shard
    starts = jnp.minimum((before // ALIGN) * ALIGN, slot_count - WINDOW)
    start_of = jnp.sum(shard_hot * starts[:, None, :], axis=2).reshape(length)
    cols = owner_all * WINDOW + slot_index - start_of
    selected = jnp.concatenate([band_rows[0], band_cols[0]], axis=1)
    bias_pair = lax.dynamic_slice_in_dim(bias, my_index * per_dev, per_dev, 0)

    cell_rows = split_heads(qkv_owned[0], num_dev, group_width)
    arrived = lax.all_to_all(cell_rows, "seq", split_axis=0, concat_axis=0, tiled=True)
    grad_parts = grad_out[0].reshape(tok_rows, num_dev, group_width).transpose(1, 0, 2)
    grad_heads = lax.all_to_all(grad_parts, "seq", split_axis=0, concat_axis=0, tiled=True)
    grad_heads = grad_heads.reshape(length, group_width)
    parts = gather_rows(arrived, starts, cols)

    attention_result, grad_rows, bias_grad = attend_fused(
        parts, grad_heads, selected, bias_pair[0], ROW_BLOCKS
    )
    bias_grad = bias_grad[None, :]

    send_back = scatter_rows(grad_rows, starts, cols, slot_count)
    returned = lax.all_to_all(send_back, "seq", split_axis=0, concat_axis=0, tiled=True)
    grad_cells = join_heads(returned)
    out_rows = lax.all_to_all(
        attention_result.reshape(num_dev, tok_rows, group_width),
        "seq",
        split_axis=0,
        concat_axis=0,
        tiled=True,
    )
    attended_rows = out_rows.transpose(1, 0, 2).reshape(tok_rows, row_width)
    bias_total = lax.psum(bias_grad, "mp")
    return (
        attended_rows.reshape(1, tok_rows, row_width),
        grad_cells.reshape(1, slot_count, features),
        bias_total,
    )


def solution(mesh):
    in_specs = (
        P("mp", "seq", None),
        P("mp", None),
        P("mp", None, None),
        P("mp", None, None),
        P(),
        P("mp", "seq", None),
    )
    out_specs = (P("mp", "seq", None), P("mp", "seq", None), P("seq", None))
    return jax.shard_map(shards, mesh=mesh, in_specs=in_specs, out_specs=out_specs, check_vma=False)
```

```python
import functools
import math

import jax
import jax.numpy as jnp
from jax import lax
from jax.experimental import pallas as pl
from jax.experimental.pallas import tpu as pltpu
from jax.sharding import PartitionSpec as P

INTERPRET = False

HEADS = 16
HEAD_DIM = 128
ROW_BLOCKS = 4


def owner_tables(owner_all, num_dev):
    owner_ids = jnp.arange(num_dev, dtype=jnp.int32)
    onehot = (owner_all[:, None] == owner_ids[None, :]).astype(jnp.int32)
    running = jnp.cumsum(onehot, axis=0) - onehot
    slot_index = jnp.sum(running * onehot, axis=1)
    return (slot_index, onehot)


def attend_head(query, key, value, grad, selected, bias_pair, row_count):
    length, head_dim = query.shape
    num_blocks, num_sel = selected.shape
    blk_rows = length // num_blocks
    score_scaling = 1.0 / math.sqrt(head_dim)

    def blocks(array):
        return array.reshape(num_blocks, blk_rows, head_dim)

    query_block = blocks(query)
    grad_block = blocks(grad)
    selected_keys = blocks(key)[selected].reshape(num_blocks, num_sel * blk_rows, head_dim)
    selected_values = blocks(value)[selected].reshape(num_blocks, num_sel * blk_rows, head_dim)
    col_kind = jnp.arange(num_sel * blk_rows) >= row_count * blk_rows
    key_offset_bias = jnp.where(col_kind, bias_pair[1], bias_pair[0])
    logit_scores = (
        jnp.einsum("bqd,bkd->bqk", query_block, selected_keys, preferred_element_type=jnp.float32)
        * score_scaling
    )
    logit_scores = logit_scores + key_offset_bias[None, None, :]
    row_max = jnp.max(logit_scores, axis=-1, keepdims=True)
    exp_scores = jnp.exp(logit_scores - row_max)
    weights = exp_scores / jnp.sum(exp_scores, axis=-1, keepdims=True)
    reduced_weights = weights.astype(jnp.bfloat16)
    attention_result = jnp.einsum(
        "bqk,bkd->bqd", reduced_weights, selected_values, preferred_element_type=jnp.float32
    ).astype(jnp.bfloat16)
    row_delta = jnp.sum(
        grad_block.astype(jnp.float32) * attention_result.astype(jnp.float32), axis=-1, keepdims=True
    )
    probability_gradient = jnp.einsum(
        "bqd,bkd->bqk", grad_block, selected_values, preferred_element_type=jnp.float32
    )
    dscore = weights * (probability_gradient - row_delta)
    bias_grad = jnp.stack(
        [jnp.sum(jnp.where(col_kind, 0.0, dscore)), jnp.sum(jnp.where(col_kind, dscore, 0.0))]
    )
    score_gradient_reduced = dscore.astype(jnp.bfloat16)
    query_gradient = (
        jnp.einsum(
            "bqk,bkd->bqd", score_gradient_reduced, selected_keys, preferred_element_type=jnp.float32
        )
        * score_scaling
    )
    selected_key_gradient = (
        jnp.einsum(
            "bqk,bqd->bkd", score_gradient_reduced, query_block, preferred_element_type=jnp.float32
        )
        * score_scaling
    )
    selected_value_gradient = jnp.einsum(
        "bqk,bqd->bkd", reduced_weights, grad_block, preferred_element_type=jnp.float32
    )
    block_hot = (
        selected[:, :, None] == jnp.arange(num_blocks, dtype=jnp.int32)[None, None, :]
    ).astype(jnp.float32)
    grad_key = jnp.einsum(
        "bjc,bjtd->ctd",
        block_hot,
        selected_key_gradient.reshape(num_blocks, num_sel, blk_rows, head_dim),
        precision=lax.Precision.HIGHEST,
    )
    grad_value = jnp.einsum(
        "bjc,bjtd->ctd",
        block_hot,
        selected_value_gradient.reshape(num_blocks, num_sel, blk_rows, head_dim),
        precision=lax.Precision.HIGHEST,
    )
    return (
        attention_result.reshape(length, head_dim),
        query_gradient.reshape(length, head_dim),
        grad_key.reshape(length, head_dim),
        grad_value.reshape(length, head_dim),
        bias_grad,
    )


def attention_kernel(row_count, sel_ref, bias_ref, qkv_ref, g_ref, o_ref, grads_ref, db_ref, dk_acc, dv_acc):
    num_blocks, num_sel = sel_ref.shape
    head_dim = g_ref.shape[1]
    blk = g_ref.shape[0] // num_blocks
    score_scaling = 1.0 / math.sqrt(head_dim)
    dk_acc[...] = jnp.zeros_like(dk_acc)
    dv_acc[...] = jnp.zeros_like(dv_acc)
    col_kind = lax.broadcasted_iota(jnp.int32, (blk, num_sel * blk), 1) >= row_count * blk
    key_offset_bias = jnp.where(col_kind, bias_ref[1], bias_ref[0])
    trans_a = (((0,), (0,)), ((), ()))
    trans_b = (((1,), (1,)), ((), ()))

    def body(b, carry):
        acc_row, acc_col = carry
        start = pl.multiple_of(b * blk, blk)
        query_block = qkv_ref[0, pl.ds(start, blk), :]
        grad_block = g_ref[pl.ds(start, blk), :]
        picks = [pl.multiple_of(sel_ref[b, i] * blk, blk) for i in range(num_sel)]
        keys = jnp.concatenate([qkv_ref[1, pl.ds(p, blk), :] for p in picks], axis=0)
        values = jnp.concatenate([qkv_ref[2, pl.ds(p, blk), :] for p in picks], axis=0)
        logits = lax.dot_general(query_block, keys, trans_b, preferred_element_type=jnp.float32)
        logits = logits * score_scaling + key_offset_bias
        row_max = jnp.max(logits, axis=1, keepdims=True)
        exp_scores = jnp.exp(logits - row_max)
        weights = exp_scores / jnp.sum(exp_scores, axis=1, keepdims=True)
        reduced_weights = weights.astype(jnp.bfloat16)
        result = jnp.dot(reduced_weights, values, preferred_element_type=jnp.float32).astype(jnp.bfloat16)
        o_ref[pl.ds(start, blk), :] = result
        row_delta = jnp.sum(
            grad_block.astype(jnp.float32) * result.astype(jnp.float32), axis=1, keepdims=True
        )
        prob_grad = lax.dot_general(grad_block, values, trans_b, preferred_element_type=jnp.float32)
        dscore = weights * (prob_grad - row_delta)
        acc_row = acc_row + jnp.sum(jnp.where(col_kind, 0.0, dscore), keepdims=True)
        acc_col = acc_col + jnp.sum(jnp.where(col_kind, dscore, 0.0), keepdims=True)
        reduced_dscore = dscore.astype(jnp.bfloat16)
        query_grad = jnp.dot(reduced_dscore, keys, preferred_element_type=jnp.float32) * score_scaling
        grads_ref[0, pl.ds(start, blk), :] = query_grad.astype(grads_ref.dtype)
        key_grad = lax.dot_general(
            reduced_dscore, query_block, trans_a, preferred_element_type=jnp.float32
        ) * score_scaling
        value_grad = lax.dot_general(
            reduced_weights, grad_block, trans_a, preferred_element_type=jnp.float32
        )
        for i, p in enumerate(picks):
            rows = pl.ds(p, blk)
            dk_acc[rows, :] += key_grad[i * blk:(i + 1) * blk]
            dv_acc[rows, :] += value_grad[i * blk:(i + 1) * blk]
        return acc_row, acc_col

    zero = jnp.zeros((1, 1), jnp.float32)
    acc_row, acc_col = lax.fori_loop(0, num_blocks, body, (zero, zero), unroll=True)
    grads_ref[1] = dk_acc[...].astype(grads_ref.dtype)
    grads_ref[2] = dv_acc[...].astype(grads_ref.dtype)
    lane = lax.broadcasted_iota(jnp.int32, db_ref.shape, 1)
    db_ref[...] = jnp.where(lane == 0, acc_row, jnp.where(lane == 1, acc_col, 0.0))


def attend_fused(parts, grad, selected, bias_pair, row_count):
    _, length, head_dim = parts.shape
    smem = pl.BlockSpec(memory_space=pltpu.SMEM)
    vmem = pl.BlockSpec(memory_space=pltpu.VMEM)
    flops = 6 * 2 * length * selected.shape[1] * (length // selected.shape[0]) * head_dim
    result, grads, bias_grad = pl.pallas_call(
        functools.partial(attention_kernel, row_count),
        in_specs=[smem, smem, vmem, vmem],
        out_specs=[vmem, vmem, vmem],
        out_shape=[
            jax.ShapeDtypeStruct((length, head_dim), jnp.bfloat16),
            jax.ShapeDtypeStruct((3, length, head_dim), jnp.bfloat16),
            jax.ShapeDtypeStruct((1, 128), jnp.float32),
        ],
        scratch_shapes=[
            pltpu.VMEM((length, head_dim), jnp.float32),
            pltpu.VMEM((length, head_dim), jnp.float32),
        ],
        cost_estimate=pl.CostEstimate(
            flops=flops, transcendentals=length * selected.shape[1] * 128, bytes_accessed=12 * length * head_dim
        ),
        interpret=INTERPRET,
    )(selected, bias_pair, parts, grad)
    return result, grads, bias_grad[0, :2]


WINDOW = 48
ALIGN = 16


def gather_kernel(starts_ref, cols_ref, cells_ref, o_ref):
    num_dev, kinds, _, _ = cells_ref.shape
    blk = cols_ref.shape[0] // num_dev

    def body(q, carry):
        begin = pl.multiple_of(q * blk, blk)
        picker = (
            lax.broadcasted_iota(jnp.int32, (blk, num_dev * WINDOW), 1) == cols_ref[pl.ds(begin, blk), :]
        ).astype(cells_ref.dtype)
        for j in range(kinds):
            window = jnp.concatenate(
                [
                    cells_ref[o, j, pl.ds(pl.multiple_of(starts_ref[q, o], ALIGN), WINDOW), :]
                    for o in range(num_dev)
                ],
                axis=0,
            )
            o_ref[j, pl.ds(begin, blk), :] = jnp.dot(
                picker, window, preferred_element_type=jnp.float32
            ).astype(o_ref.dtype)
        return carry

    lax.fori_loop(0, num_dev, body, 0, unroll=True)


def gather_rows(cells, starts, cols):
    num_dev, kinds, slot_count, width = cells.shape
    length = cols.shape[0]
    smem = pl.BlockSpec(memory_space=pltpu.SMEM)
    vmem = pl.BlockSpec(memory_space=pltpu.VMEM)
    return pl.pallas_call(
        gather_kernel,
        in_specs=[smem, vmem, vmem],
        out_specs=vmem,
        out_shape=jax.ShapeDtypeStruct((kinds, length, width), cells.dtype),
        cost_estimate=pl.CostEstimate(
            flops=2 * kinds * length * num_dev * WINDOW * width,
            transcendentals=0,
            bytes_accessed=2 * (cells.size + kinds * length * width),
        ),
        interpret=INTERPRET,
    )(starts, cols.reshape(length, 1), cells)


def scatter_kernel(starts_ref, cols_ref, grads_ref, o_ref, acc):
    num_dev = starts_ref.shape[0]
    kinds, length, width = grads_ref.shape
    blk = length // num_dev
    acc[...] = jnp.zeros_like(acc)

    def body(q, carry):
        spread = (
            lax.broadcasted_iota(jnp.int32, (num_dev * WINDOW, blk), 0) == cols_ref[pl.ds(q, 1), :]
        ).astype(grads_ref.dtype)
        begin = pl.multiple_of(q * blk, blk)
        for j in range(kinds):
            placed = jnp.dot(spread, grads_ref[j, pl.ds(begin, blk), :], preferred_element_type=jnp.float32)
            for o in range(num_dev):
                rows = pl.ds(pl.multiple_of(starts_ref[q, o], ALIGN), WINDOW)
                acc[o, j, rows, :] += placed[o * WINDOW:(o + 1) * WINDOW]
        return carry

    lax.fori_loop(0, num_dev, body, 0, unroll=True)
    o_ref[...] = acc[...].astype(o_ref.dtype)


def scatter_rows(grads, starts, cols, slot_count):
    kinds, length, width = grads.shape
    num_dev = starts.shape[0]
    smem = pl.BlockSpec(memory_space=pltpu.SMEM)
    vmem = pl.BlockSpec(memory_space=pltpu.VMEM)
    return pl.pallas_call(
        scatter_kernel,
        in_specs=[smem, vmem, vmem],
        out_specs=vmem,
        out_shape=jax.ShapeDtypeStruct((num_dev, kinds, slot_count, width), grads.dtype),
        scratch_shapes=[pltpu.VMEM((num_dev, kinds, slot_count, width), jnp.float32)],
        cost_estimate=pl.CostEstimate(
            flops=2 * kinds * length * num_dev * WINDOW * width,
            transcendentals=0,
            bytes_accessed=2 * (grads.size + num_dev * kinds * slot_count * width),
        ),
        interpret=INTERPRET,
    )(starts, cols.reshape(num_dev, length // num_dev), grads)


def split_heads(cells, num_dev, group_width):
    slot_count, features = cells.shape
    span = num_dev * group_width

    def body(x_ref, o_ref):
        for h in range(num_dev):
            o_ref[h, 0] = x_ref[:, h * group_width:(h + 1) * group_width]

    return pl.pallas_call(
        body,
        grid=(features // span,),
        in_specs=[pl.BlockSpec((slot_count, span), lambda j: (0, j))],
        out_specs=pl.BlockSpec((num_dev, 1, slot_count, group_width), lambda j: (0, j, 0, 0)),
        out_shape=jax.ShapeDtypeStruct((num_dev, features // span, slot_count, group_width), cells.dtype),
        interpret=INTERPRET,
    )(cells)


def join_heads(parts):
    num_dev, kinds, slot_count, group_width = parts.shape
    span = num_dev * group_width

    def body(x_ref, o_ref):
        for h in range(num_dev):
            o_ref[:, h * group_width:(h + 1) * group_width] = x_ref[h, 0]

    return pl.pallas_call(
        body,
        grid=(kinds,),
        in_specs=[pl.BlockSpec((num_dev, 1, slot_count, group_width), lambda j: (0, j, 0, 0))],
        out_specs=pl.BlockSpec((slot_count, span), lambda j: (0, j)),
        out_shape=jax.ShapeDtypeStruct((slot_count, kinds * span), parts.dtype),
        interpret=INTERPRET,
    )(parts)


def shards(qkv_owned, owner, band_rows, band_cols, bias, grad_out):
    num_dev = lax.axis_size("seq")
    my_index = lax.axis_index("seq")
    slot_count = qkv_owned.shape[1]
    features = qkv_owned.shape[2]
    tok_rows = grad_out.shape[1]
    row_width = grad_out.shape[2]
    per_dev = HEADS // num_dev
    group_width = per_dev * HEAD_DIM
    length = tok_rows * num_dev
    owner_all = owner[0]
    slot_index, onehot = owner_tables(owner_all, num_dev)
    shard_hot = onehot.reshape(num_dev, tok_rows, num_dev)
    per_shard = jnp.sum(shard_hot, axis=1)
    before = jnp.cumsum(per_shard, axis=0) - per_shard
    starts = jnp.minimum((before // ALIGN) * ALIGN, slot_count - WINDOW)
    start_of = jnp.sum(shard_hot * starts[:, None, :], axis=2).reshape(length)
    cols = owner_all * WINDOW + slot_index - start_of
    selected = jnp.concatenate([band_rows[0], band_cols[0]], axis=1)
    bias_pair = lax.dynamic_slice_in_dim(bias, my_index * per_dev, per_dev, 0)

    cell_rows = split_heads(qkv_owned[0], num_dev, group_width)
    arrived = lax.all_to_all(cell_rows, "seq", split_axis=0, concat_axis=0, tiled=True)
    grad_parts = grad_out[0].reshape(tok_rows, num_dev, group_width).transpose(1, 0, 2)
    grad_heads = lax.all_to_all(grad_parts, "seq", split_axis=0, concat_axis=0, tiled=True)
    grad_heads = grad_heads.reshape(length, group_width)
    parts = gather_rows(arrived, starts, cols)

    attention_result, grad_rows, bias_grad = attend_fused(
        parts, grad_heads, selected, bias_pair[0], ROW_BLOCKS
    )
    bias_grad = bias_grad[None, :]

    send_back = scatter_rows(grad_rows, starts, cols, slot_count)
    returned = lax.all_to_all(send_back, "seq", split_axis=0, concat_axis=0, tiled=True)
    grad_cells = join_heads(returned)
    out_rows = lax.all_to_all(
        attention_result.reshape(num_dev, tok_rows, group_width),
        "seq",
        split_axis=0,
        concat_axis=0,
        tiled=True,
    )
    attended_rows = out_rows.transpose(1, 0, 2).reshape(tok_rows, row_width)
    bias_total = lax.psum(bias_grad, "mp")
    return (
        attended_rows.reshape(1, tok_rows, row_width),
        grad_cells.reshape(1, slot_count, features),
        bias_total,
    )


def solution(mesh):
    in_specs = (
        P("mp", "seq", None),
        P("mp", None),
        P("mp", None, None),
        P("mp", None, None),
        P(),
        P("mp", "seq", None),
    )
    out_specs = (P("mp", "seq", None), P("mp", "seq", None), P("seq", None))
    return jax.shard_map(shards, mesh=mesh, in_specs=in_specs, out_specs=out_specs, check_vma=False)
```
